512 devices in a mesh: blk: 32 (over y, z_lo), band: 16 (over z_hi, x, core).
Axes of the slice: x: 4, y: 4, z: 16 (z_hi: 2, z_lo: 8; z = z_hi * 8 + z_lo), core: 2. Of those that a mesh axis runs over, the one named last changes fastest.
Arguments:
- spectra: bfloat16 [1024, 4, 2, 2048], P('blk', None, None, 'band'), may hold values from -1800 to 1800
- live: int32 [1024, 4], P('blk'), may hold values 0 or 1
- pair_table: int32 [32, 32], P('blk'), may hold values 0 or 1
Outputs:
- correlations: float32 [16, 1024, 32, 1024], P('band', 'blk')
The draws below stay inside these ranges and needn't reach their ends.
All inputs are finite; a program needn't handle non-finite values. No bound on the sum of `live` or of `pair_table` on one device may be relied on, other than what follows from the above.
Results may differ from the reference program's by a relative error of at most 0.005.
Values may be sent and summed in bfloat16 or wider, within the bound.
No kernel may reach another device: no remote copies, remote signals or barrier semaphores. Data moves between devices by JAX's collectives and lax.ppermute only.
A program may use at most 128 MiB of HBM per device.

```python
import math
import jax
import jax.numpy as jnp
from jax import lax

CH_DEV = 32
WINDOWS = 4
LAGS = 32
FREQ_BINS = 2048
SMOOTH = 32
CHANNELS = 1024
BLOCKS = 32
FB_DEV = 128
N_BAND = 16


def draw_spectra(key, part):
    keys = jax.random.split(key, 5)
    shape = (CHANNELS, WINDOWS, 2, FREQ_BINS)
    channel_gain = jnp.exp(jax.random.uniform(keys[0], (CHANNELS, 1, 1, 1), jnp.float32, 0.0, math.log(10.0)))
    window_gain = jnp.exp(jax.random.uniform(keys[1], (1, WINDOWS, 1, 1), jnp.float32, 0.0, math.log(3.0)))
    bin_gain = jnp.exp(jax.random.uniform(keys[2], (1, 1, 1, FREQ_BINS), jnp.float32, 0.0, math.log(10.0)))
    base = jax.random.truncated_normal(keys[4], -6.0, 6.0, shape, jnp.float32)
    return (base * channel_gain * window_gain * bin_gain).astype(jnp.bfloat16)


def set_ends(entries, stream_key, least, largest):
    dims = entries.shape
    index_at = [jax.random.randint(jax.random.fold_in(stream_key, axis), (), 0, dims[axis]) for axis in range(len(dims))]
    entries = entries.at[tuple(index_at)].set(least)
    longest = dims.index(max(dims))
    index_at[longest] = (index_at[longest] + 1) % dims[longest]
    return entries.at[tuple(index_at)].set(largest)


def setup_inputs(seed: int = 0) -> dict:
    streams_of = jax.random.split(jax.random.key(seed), 4)
    return {
        "spectra": draw_spectra(jax.random.fold_in(streams_of[3], 71), 0),
        "live": set_ends((jax.random.randint(streams_of[1], (CHANNELS, WINDOWS), 0, 4) < 3).astype(jnp.int32), jax.random.fold_in(streams_of[1], 1), 0, 1),
        "pair_table": set_ends((jax.random.randint(streams_of[2], (BLOCKS, BLOCKS), 0, 4) < 3).astype(jnp.int32), jax.random.fold_in(streams_of[2], 1), 0, 1),
    }


EPSILON = 1e-06

def reference(spectra, live, pair_table):
    values = spectra.astype(jnp.float32)
    real_part = values[:, :, 0, :]
    imag_part = values[:, :, 1, :]
    amplitude = jnp.sqrt(real_part * real_part + imag_part * imag_part)
    padded = jnp.pad(amplitude, ((0, 0), (0, 0), (SMOOTH, SMOOTH)))
    total = jnp.zeros_like(amplitude)
    for offset in range(2 * SMOOTH + 1):
        total = total + padded[:, :, offset:offset + FREQ_BINS]
    indices = jnp.arange(FREQ_BINS, dtype=jnp.int32)
    covered = (jnp.minimum(indices + SMOOTH, FREQ_BINS - 1) - jnp.maximum(indices - SMOOTH, 0) + 1).astype(jnp.float32)
    smooth = total / covered
    factor = live.astype(jnp.float32)[:, :, None] / (smooth + EPSILON)
    white = (values * factor[:, :, None, :]).astype(jnp.bfloat16)
    alive = live.astype(jnp.float32)
    count = jnp.dot(alive, alive.T, precision=lax.Precision.HIGHEST, preferred_element_type=jnp.float32)
    keep = jnp.repeat(jnp.repeat(pair_table, CH_DEV, axis=0), CH_DEV, axis=1).astype(jnp.float32)
    apart = 1.0 - jnp.eye(CHANNELS, dtype=jnp.float32)
    weight = keep * apart / jnp.sqrt(FB_DEV * jnp.maximum(count, 1.0))
    lag_index = 2 * jnp.arange(LAGS, dtype=jnp.int32) + 1 - LAGS
    results = []
    for band_number in range(N_BAND):
        first = band_number * FB_DEV
        band_bins = indices[first:first + FB_DEV]
        phase = (lag_index[:, None] * band_bins[None, :]).astype(jnp.float32) * (math.pi / FREQ_BINS)
        cosine = jnp.cos(phase)[None, :, None, :]
        sine = jnp.sin(phase)[None, :, None, :]
        section = white[:, :, :, first:first + FB_DEV]
        white_real = section[:, :, 0, :].astype(jnp.float32)[:, None]
        white_imag = section[:, :, 1, :].astype(jnp.float32)[:, None]
        rot_real = white_real * cosine - white_imag * sine
        rot_imag = white_real * sine + white_imag * cosine
        rotated = jnp.stack([rot_real, rot_imag], axis=3).astype(jnp.bfloat16).reshape(CHANNELS * LAGS, -1)
        columns = section.reshape(CHANNELS, -1)
        product = lax.dot_general(rotated, columns, (((1,), (1,)), ((), ())), preferred_element_type=jnp.float32)
        product = product.reshape(CHANNELS, LAGS, CHANNELS)
        results.append(product * weight[:, None, :])
    return jnp.stack(results, axis=0)
```

```python
import math

import jax
import jax.numpy as jnp
from jax import lax
from jax.sharding import PartitionSpec as P

LAGS = 32
FREQ_BINS = 2048
SMOOTH = 32


EPSILON = 1e-06


def padded_2(cells, sides, width):
    for axis, dim in sides:
        count = lax.axis_size(axis)
        ends = count - 1
        head = lax.slice_in_dim(cells, 0, width, axis=dim)
        tail = lax.slice_in_dim(cells, cells.shape[dim] - width, cells.shape[dim], axis=dim)
        cells = jnp.concatenate(
            [
                lax.ppermute(tail, axis, [(i, (i + 1) % count) for i in range(ends)]),
                cells,
                lax.ppermute(head, axis, [((i + 1) % count, i) for i in range(ends)]),
            ],
            axis=dim,
        )
    return cells


def shards(spectra, live, pair_table):
    home_rows = spectra.shape[0]
    windows = spectra.shape[1]
    bins_dev = spectra.shape[3]
    blocks_total = lax.axis_size("blk")
    me_block = lax.axis_index("blk")
    first_row = me_block * home_rows
    channels = blocks_total * home_rows
    values = spectra.astype(jnp.float32)
    real_part = values[:, :, 0, :]
    imag_part = values[:, :, 1, :]
    amplitude = jnp.sqrt(real_part * real_part + imag_part * imag_part)
    padded = padded_2(amplitude, (("band", 2),), SMOOTH)
    wide_bins = bins_dev + 2 * SMOOTH
    source_bin = jnp.arange(wide_bins, dtype=jnp.int32)[:, None]
    target_bin = jnp.arange(bins_dev, dtype=jnp.int32)[None, :]
    window_matrix = ((source_bin >= target_bin) & (source_bin <= target_bin + 2 * SMOOTH)).astype(
        jnp.float32
    )
    total = jnp.dot(
        padded.reshape(home_rows * windows, wide_bins),
        window_matrix,
        precision=lax.Precision.HIGHEST,
        preferred_element_type=jnp.float32,
    )
    total = total.reshape(home_rows, windows, bins_dev)
    indices = lax.axis_index("band") * bins_dev + jnp.arange(bins_dev, dtype=jnp.int32)
    covered = (
        jnp.minimum(indices + SMOOTH, FREQ_BINS - 1) - jnp.maximum(indices - SMOOTH, 0) + 1
    ).astype(jnp.float32)
    smooth = total / covered
    factor = live.astype(jnp.float32)[:, :, None] / (smooth + EPSILON)
    white = (values * factor[:, :, None, :]).astype(jnp.bfloat16)
    lag_index = 2 * jnp.arange(LAGS, dtype=jnp.int32) + 1 - LAGS
    phase = (lag_index[:, None] * indices[None, :]).astype(jnp.float32) * (math.pi / FREQ_BINS)
    cosine = jnp.cos(phase)[None, :, None, :]
    sine = jnp.sin(phase)[None, :, None, :]
    white_real = white[:, :, 0, :].astype(jnp.float32)[:, None]
    white_imag = white[:, :, 1, :].astype(jnp.float32)[:, None]
    rot_real = white_real * cosine - white_imag * sine
    rot_imag = white_real * sine + white_imag * cosine
    zeta = (
        jnp.stack([rot_real, rot_imag], axis=3).astype(jnp.bfloat16).reshape(home_rows * LAGS, -1)
    )

    white_all = lax.all_gather(white.reshape(home_rows, -1), "blk", axis=0, tiled=True)
    live_all = lax.all_gather(live, "blk", axis=0, tiled=True)

    product = lax.dot_general(
        zeta,
        white_all,
        (((1,), (1,)), ((), ())),
        preferred_element_type=jnp.float32,
    )
    product = product.reshape(home_rows, LAGS, channels)
    count = lax.dot_general(
        live.astype(jnp.float32),
        live_all.astype(jnp.float32),
        (((1,), (1,)), ((), ())),
        precision=lax.Precision.HIGHEST,
        preferred_element_type=jnp.float32,
    )
    keep = jnp.broadcast_to(pair_table[0][:, None], (blocks_total, home_rows)).reshape(channels)
    rows_global = first_row + jnp.arange(home_rows, dtype=jnp.int32)
    columns = jnp.arange(channels, dtype=jnp.int32)
    apart = (rows_global[:, None] != columns[None, :]).astype(jnp.float32)
    weight = keep.astype(jnp.float32)[None, :] * apart / jnp.sqrt(bins_dev * jnp.maximum(count, 1.0))
    result = product * weight[:, None, :]
    return result[None]


def solution(mesh):
    in_specs = (P("blk", None, None, "band"), P("blk", None), P("blk", None))
    out_specs = P("band", "blk", None, None)
    return jax.shard_map(shards, mesh=mesh, in_specs=in_specs, out_specs=out_specs, check_vma=False)
```

```python
import math

import jax
import jax.numpy as jnp
from jax import lax
from jax.sharding import Mesh, PartitionSpec as P

LAGS = 32
FREQ_BINS = 2048
SMOOTH = 32


EPSILON = 1e-06
BLK = ("by", "bz")
BAND = ("nz", "nx", "nc")


def padded_2(cells, sides, width):
    for axis, dim in sides:
        count = lax.axis_size(axis)
        ends = count - 1
        head = lax.slice_in_dim(cells, 0, width, axis=dim)
        tail = lax.slice_in_dim(cells, cells.shape[dim] - width, cells.shape[dim], axis=dim)
        cells = jnp.concatenate(
            [
                lax.ppermute(tail, axis, [(i, (i + 1) % count) for i in range(ends)]),
                cells,
                lax.ppermute(head, axis, [((i + 1) % count, i) for i in range(ends)]),
            ],
            axis=dim,
        )
    return cells


def shards(spectra, live, pair_table):
    home_rows = spectra.shape[0]
    windows = spectra.shape[1]
    bins_dev = spectra.shape[3]
    blocks_total = lax.axis_size(BLK)
    me_block = lax.axis_index(BLK)
    first_row = me_block * home_rows
    channels = blocks_total * home_rows
    values = spectra.astype(jnp.float32)
    real_part = values[:, :, 0, :]
    imag_part = values[:, :, 1, :]
    amplitude = jnp.sqrt(real_part * real_part + imag_part * imag_part)
    padded = padded_2(amplitude, ((BAND, 2),), SMOOTH)
    wide_bins = bins_dev + 2 * SMOOTH
    source_bin = jnp.arange(wide_bins, dtype=jnp.int32)[:, None]
    target_bin = jnp.arange(bins_dev, dtype=jnp.int32)[None, :]
    window_matrix = ((source_bin >= target_bin) & (source_bin <= target_bin + 2 * SMOOTH)).astype(
        jnp.float32
    )
    total = jnp.dot(
        padded.reshape(home_rows * windows, wide_bins),
        window_matrix,
        precision=lax.Precision.HIGHEST,
        preferred_element_type=jnp.float32,
    )
    total = total.reshape(home_rows, windows, bins_dev)
    indices = lax.axis_index(BAND) * bins_dev + jnp.arange(bins_dev, dtype=jnp.int32)
    covered = (
        jnp.minimum(indices + SMOOTH, FREQ_BINS - 1) - jnp.maximum(indices - SMOOTH, 0) + 1
    ).astype(jnp.float32)
    smooth = total / covered
    factor = live.astype(jnp.float32)[:, :, None] / (smooth + EPSILON)
    white = (values * factor[:, :, None, :]).astype(jnp.bfloat16)
    lag_index = 2 * jnp.arange(LAGS, dtype=jnp.int32) + 1 - LAGS
    phase = (lag_index[:, None] * indices[None, :]).astype(jnp.float32) * (math.pi / FREQ_BINS)
    cosine = jnp.cos(phase)[None, :, None, :]
    sine = jnp.sin(phase)[None, :, None, :]
    white_real = white[:, :, 0, :].astype(jnp.float32)[:, None]
    white_imag = white[:, :, 1, :].astype(jnp.float32)[:, None]
    rot_real = white_real * cosine - white_imag * sine
    rot_imag = white_real * sine + white_imag * cosine
    zeta = (
        jnp.stack([rot_real, rot_imag], axis=3).astype(jnp.bfloat16).reshape(home_rows * LAGS, -1)
    )

    marks = jnp.zeros((home_rows, bins_dev), jnp.bfloat16).at[:, :windows].set(live.astype(jnp.bfloat16))
    parcel = jnp.concatenate([white.reshape(home_rows, windows * 2, bins_dev), marks[:, None]], axis=1)
    parcel = lax.all_gather(parcel[None], "by", axis=0, tiled=True)
    parcel = lax.all_gather(parcel[None], "bz", axis=0, tiled=True)
    parcel = jnp.transpose(parcel, (1, 0, 2, 3, 4)).reshape(channels, windows * 2 + 1, bins_dev)
    white_all = parcel[:, : windows * 2].reshape(channels, -1)
    live_all = parcel[:, windows * 2, :windows]

    product = lax.dot_general(
        zeta,
        white_all,
        (((1,), (1,)), ((), ())),
        preferred_element_type=jnp.float32,
    )
    product = product.reshape(home_rows, LAGS, channels)
    count = lax.dot_general(
        live.astype(jnp.float32),
        live_all.astype(jnp.float32),
        (((1,), (1,)), ((), ())),
        precision=lax.Precision.HIGHEST,
        preferred_element_type=jnp.float32,
    )
    keep = jnp.broadcast_to(pair_table[0][:, None], (blocks_total, home_rows)).reshape(channels)
    rows_global = first_row + jnp.arange(home_rows, dtype=jnp.int32)
    columns = jnp.arange(channels, dtype=jnp.int32)
    apart = (rows_global[:, None] != columns[None, :]).astype(jnp.float32)
    weight = keep.astype(jnp.float32)[None, :] * apart / jnp.sqrt(bins_dev * jnp.maximum(count, 1.0))
    result = product * weight[:, None, :]
    return result[None]


def solution(mesh):
    blk_size, band_size = mesh.devices.shape
    fine = Mesh(mesh.devices.reshape(4, blk_size // 4, 2, band_size // 4, 2), BLK + BAND)
    in_specs = (P(BLK, None, None, BAND), P(BLK, None), P(BLK, None))
    out_specs = P(BAND, BLK, None, None)
    return jax.shard_map(shards, mesh=fine, in_specs=in_specs, out_specs=out_specs, check_vma=False)
```

```python
import math

import jax
import jax.numpy as jnp
from jax import lax
from jax.sharding import Mesh, PartitionSpec as P

LAGS = 32
FREQ_BINS = 2048
SMOOTH = 32


EPSILON = 1e-06
BLK = ("by", "bz")
BAND = ("nz", "nx", "nc")


def padded_2(cells, sides, width):
    for axis, dim in sides:
        count = lax.axis_size(axis)
        ends = count - 1
        head = lax.slice_in_dim(cells, 0, width, axis=dim)
        tail = lax.slice_in_dim(cells, cells.shape[dim] - width, cells.shape[dim], axis=dim)
        cells = jnp.concatenate(
            [
                lax.ppermute(tail, axis, [(i, (i + 1) % count) for i in range(ends)]),
                cells,
                lax.ppermute(head, axis, [((i + 1) % count, i) for i in range(ends)]),
            ],
            axis=dim,
        )
    return cells


def shards(spectra, live, pair_table):
    home_rows = spectra.shape[0]
    windows = spectra.shape[1]
    bins_dev = spectra.shape[3]
    blocks_total = lax.axis_size(BLK)
    me_block = lax.axis_index(BLK)
    first_row = me_block * home_rows
    channels = blocks_total * home_rows
    values = spectra.astype(jnp.float32)
    real_part = values[:, :, 0, :]
    imag_part = values[:, :, 1, :]
    amplitude = jnp.sqrt(real_part * real_part + imag_part * imag_part)
    padded = padded_2(amplitude, ((BAND, 2),), SMOOTH)
    wide_bins = bins_dev + 2 * SMOOTH
    source_bin = jnp.arange(wide_bins, dtype=jnp.int32)[:, None]
    target_bin = jnp.arange(bins_dev, dtype=jnp.int32)[None, :]
    window_matrix = ((source_bin >= target_bin) & (source_bin <= target_bin + 2 * SMOOTH)).astype(
        jnp.float32
    )
    total = jnp.dot(
        padded.reshape(home_rows * windows, wide_bins),
        window_matrix,
        precision=lax.Precision.HIGHEST,
        preferred_element_type=jnp.float32,
    )
    total = total.reshape(home_rows, windows, bins_dev)
    indices = lax.axis_index(BAND) * bins_dev + jnp.arange(bins_dev, dtype=jnp.int32)
    covered = (
        jnp.minimum(indices + SMOOTH, FREQ_BINS - 1) - jnp.maximum(indices - SMOOTH, 0) + 1
    ).astype(jnp.float32)
    smooth = total / covered
    factor = live.astype(jnp.float32)[:, :, None] / (smooth + EPSILON)
    white = (values * factor[:, :, None, :]).astype(jnp.bfloat16)
    lag_index = 2 * jnp.arange(LAGS, dtype=jnp.int32) + 1 - LAGS
    phase = (lag_index[:, None] * indices[None, :]).astype(jnp.float32) * (math.pi / FREQ_BINS)
    cosine = jnp.cos(phase)[None, :, None, :]
    sine = jnp.sin(phase)[None, :, None, :]
    white_real = white[:, :, 0, :].astype(jnp.float32)[:, None]
    white_imag = white[:, :, 1, :].astype(jnp.float32)[:, None]
    rot_real = white_real * cosine - white_imag * sine
    rot_imag = white_real * sine + white_imag * cosine
    zeta = (
        jnp.stack([rot_real, rot_imag], axis=3).astype(jnp.bfloat16).reshape(home_rows * LAGS, -1)
    )

    marks = jnp.zeros((home_rows, bins_dev), jnp.bfloat16).at[:, :windows].set(live.astype(jnp.bfloat16))
    parcel = jnp.concatenate([white.reshape(home_rows, windows * 2, bins_dev), marks[:, None]], axis=1)
    slots = parcel.shape[1]
    row_span = exchanged_on_line(parcel, "bz").reshape(-1, slots, bins_dev)
    ring = lax.axis_size("by")
    me_ring = lax.axis_index("by")
    span = row_span.shape[0]
    half = span // 2
    from_lo = shifted(row_span, "by", 1)
    from_hi = shifted(row_span, "by", -1)
    far = jnp.concatenate(
        [shifted(from_lo[:half], "by", 1), shifted(from_hi[half:], "by", -1)], axis=0
    )
    zeta_wide = jnp.concatenate(
        [zeta.reshape(home_rows * LAGS, windows * 2, bins_dev),
         jnp.zeros((home_rows * LAGS, 1, bins_dev), jnp.bfloat16)],
        axis=1,
    ).reshape(home_rows * LAGS, -1)
    live_home = live.astype(jnp.float32)
    keep_all = jnp.broadcast_to(pair_table[0][:, None], (blocks_total, home_rows)).reshape(channels)
    keep_all = keep_all.astype(jnp.float32)
    rows_global = first_row + jnp.arange(home_rows, dtype=jnp.int32)
    result = jnp.zeros((home_rows, LAGS, channels), jnp.float32)
    for offset, chunk in ((0, row_span), (1, from_hi), (2, far), (ring - 1, from_lo)):
        place = ((me_ring + offset) % ring) * span
        product = lax.dot_general(
            zeta_wide,
            chunk.reshape(span, -1),
            (((1,), (1,)), ((), ())),
            preferred_element_type=jnp.float32,
        )
        count = lax.dot_general(
            live_home,
            chunk[:, windows * 2, :windows].astype(jnp.float32),
            (((1,), (1,)), ((), ())),
            precision=lax.Precision.HIGHEST,
            preferred_element_type=jnp.float32,
        )
        columns = place + jnp.arange(span, dtype=jnp.int32)
        keep = lax.dynamic_slice_in_dim(keep_all, place, span)
        apart = (rows_global[:, None] != columns[None, :]).astype(jnp.float32)
        weight = keep[None, :] * apart / jnp.sqrt(bins_dev * jnp.maximum(count, 1.0))
        piece = product.reshape(home_rows, LAGS, span) * weight[:, None, :]
        result = lax.dynamic_update_slice(result, piece, (0, 0, place))
    return result[None]


def shifted(value, axis, steps):
    count = lax.axis_size(axis)
    return lax.ppermute(value, axis, [(i, (i + steps) % count) for i in range(count)])


def exchanged_on_line(value, axis):
    count = lax.axis_size(axis)
    me = lax.axis_index(axis)
    held = value[None]
    stride = 1
    while stride < count:
        other = lax.ppermute(held, axis, [(i, i ^ stride) for i in range(count)])
        low = (me // stride) % 2 == 0
        held = jnp.concatenate(
            [jnp.where(low, held, other), jnp.where(low, other, held)], axis=0
        )
        stride *= 2
    return held


def solution(mesh):
    blk_size, band_size = mesh.devices.shape
    fine = Mesh(mesh.devices.reshape(4, blk_size // 4, 2, band_size // 4, 2), BLK + BAND)
    in_specs = (P(BLK, None, None, BAND), P(BLK, None), P(BLK, None))
    out_specs = P(BAND, BLK, None, None)
    return jax.shard_map(shards, mesh=fine, in_specs=in_specs, out_specs=out_specs, check_vma=False)
```

```python
import math

import jax
import jax.numpy as jnp
from jax import lax
from jax.sharding import Mesh, PartitionSpec as P

LAGS = 32
FREQ_BINS = 2048
SMOOTH = 32


EPSILON = 1e-06
BLK = ("by", "bz")
BAND = ("nz", "nx", "nc")


def padded_2(cells, sides, width):
    for axis, dim in sides:
        count = lax.axis_size(axis)
        ends = count - 1
        head = lax.slice_in_dim(cells, 0, width, axis=dim)
        tail = lax.slice_in_dim(cells, cells.shape[dim] - width, cells.shape[dim], axis=dim)
        cells = jnp.concatenate(
            [
                lax.ppermute(tail, axis, [(i, (i + 1) % count) for i in range(ends)]),
                cells,
                lax.ppermute(head, axis, [((i + 1) % count, i) for i in range(ends)]),
            ],
            axis=dim,
        )
    return cells


def shards(spectra, live, pair_table):
    home_rows = spectra.shape[0]
    windows = spectra.shape[1]
    bins_dev = spectra.shape[3]
    blocks_total = lax.axis_size(BLK)
    me_block = lax.axis_index(BLK)
    first_row = me_block * home_rows
    channels = blocks_total * home_rows
    values = spectra.astype(jnp.float32)
    real_part = values[:, :, 0, :]
    imag_part = values[:, :, 1, :]
    amplitude = jnp.sqrt(real_part * real_part + imag_part * imag_part)
    padded = padded_2(amplitude, ((BAND, 2),), SMOOTH)
    wide_bins = bins_dev + 2 * SMOOTH
    source_bin = jnp.arange(wide_bins, dtype=jnp.int32)[:, None]
    target_bin = jnp.arange(bins_dev, dtype=jnp.int32)[None, :]
    window_matrix = ((source_bin >= target_bin) & (source_bin <= target_bin + 2 * SMOOTH)).astype(
        jnp.float32
    )
    total = jnp.dot(
        padded.reshape(home_rows * windows, wide_bins),
        window_matrix,
        precision=lax.Precision.HIGHEST,
        preferred_element_type=jnp.float32,
    )
    total = total.reshape(home_rows, windows, bins_dev)
    indices = lax.axis_index(BAND) * bins_dev + jnp.arange(bins_dev, dtype=jnp.int32)
    covered = (
        jnp.minimum(indices + SMOOTH, FREQ_BINS - 1) - jnp.maximum(indices - SMOOTH, 0) + 1
    ).astype(jnp.float32)
    smooth = total / covered
    factor = live.astype(jnp.float32)[:, :, None] / (smooth + EPSILON)
    white = (values * factor[:, :, None, :]).astype(jnp.bfloat16)
    lag_index = 2 * jnp.arange(LAGS, dtype=jnp.int32) + 1 - LAGS
    phase = (lag_index[:, None] * indices[None, :]).astype(jnp.float32) * (math.pi / FREQ_BINS)
    cosine = jnp.cos(phase)[None, :, None, :]
    sine = jnp.sin(phase)[None, :, None, :]
    white_real = white[:, :, 0, :].astype(jnp.float32)[:, None]
    white_imag = white[:, :, 1, :].astype(jnp.float32)[:, None]
    rot_real = white_real * cosine - white_imag * sine
    rot_imag = white_real * sine + white_imag * cosine
    zeta_wide = jnp.pad(
        jnp.stack([rot_real, rot_imag], axis=3).reshape(home_rows * LAGS, windows * 2, bins_dev),
        ((0, 0), (0, 1), (0, 0)),
    ).astype(jnp.bfloat16).reshape(home_rows * LAGS, -1)

    marks = jnp.zeros((home_rows, bins_dev), jnp.bfloat16).at[:, :windows].set(live.astype(jnp.bfloat16))
    parcel = jnp.concatenate([white.reshape(home_rows, windows * 2, bins_dev), marks[:, None]], axis=1)
    slots = parcel.shape[1]
    line = lax.axis_size("bz")
    me_line = lax.axis_index("bz")
    group = line // 2
    near = exchanged_on_line(parcel, "bz", group).reshape(-1, slots, bins_dev)
    other = lax.ppermute(near, "bz", [(i, i ^ group) for i in range(line)])
    ring = lax.axis_size("by")
    me_ring = lax.axis_index("by")
    span = near.shape[0]
    row_width = span * 2
    live_home = live.astype(jnp.float32)
    keep_all = jnp.broadcast_to(pair_table[0][:, None], (blocks_total, home_rows)).reshape(channels)
    keep_all = keep_all.astype(jnp.float32)
    rows_global = first_row + jnp.arange(home_rows, dtype=jnp.int32)
    result = jnp.zeros((home_rows, LAGS, channels), jnp.float32)
    my_half = (me_line // group) % 2
    for which, held in ((my_half, near), (1 - my_half, other)):
        for offset, chunk in relayed_on_ring(held, "by"):
            place = ((me_ring + offset) % ring) * row_width + which * span
            product = lax.dot_general(
                zeta_wide,
                chunk.reshape(span, -1),
                (((1,), (1,)), ((), ())),
                preferred_element_type=jnp.float32,
            )
            count = lax.dot_general(
                live_home,
                chunk[:, windows * 2, :windows].astype(jnp.float32),
                (((1,), (1,)), ((), ())),
                precision=lax.Precision.HIGHEST,
                preferred_element_type=jnp.float32,
            )
            columns = place + jnp.arange(span, dtype=jnp.int32)
            keep = lax.dynamic_slice_in_dim(keep_all, place, span)
            apart = (rows_global[:, None] != columns[None, :]).astype(jnp.float32)
            weight = keep[None, :] * apart / jnp.sqrt(bins_dev * jnp.maximum(count, 1.0))
            piece = product.reshape(home_rows, LAGS, span) * weight[:, None, :]
            result = lax.dynamic_update_slice(result, piece, (0, 0, place))
    return result[None]


def relayed_on_ring(chunk, axis):
    half = chunk.shape[0] // 2
    from_lo = shifted(chunk, axis, 1)
    from_hi = shifted(chunk, axis, -1)
    far = jnp.concatenate(
        [shifted(from_lo[:half], axis, 1), shifted(from_hi[half:], axis, -1)], axis=0
    )
    return ((0, chunk), (1, from_hi), (2, far), (lax.axis_size(axis) - 1, from_lo))


def shifted(value, axis, steps):
    count = lax.axis_size(axis)
    return lax.ppermute(value, axis, [(i, (i + steps) % count) for i in range(count)])


def exchanged_on_line(value, axis, count):
    me = lax.axis_index(axis)
    held = value[None]
    stride = 1
    while stride < count:
        other = lax.ppermute(held, axis, [(i, i ^ stride) for i in range(lax.axis_size(axis))])
        low = (me // stride) % 2 == 0
        held = jnp.concatenate(
            [jnp.where(low, held, other), jnp.where(low, other, held)], axis=0
        )
        stride *= 2
    return held


def solution(mesh):
    blk_size, band_size = mesh.devices.shape
    fine = Mesh(mesh.devices.reshape(4, blk_size // 4, 2, band_size // 4, 2), BLK + BAND)
    in_specs = (P(BLK, None, None, BAND), P(BLK, None), P(BLK, None))
    out_specs = P(BAND, BLK, None, None)
    return jax.shard_map(shards, mesh=fine, in_specs=in_specs, out_specs=out_specs, check_vma=False)
```

```python
import math

import jax
import jax.numpy as jnp
from jax import lax
from jax.sharding import Mesh, PartitionSpec as P

LAGS = 32
FREQ_BINS = 2048
SMOOTH = 32


EPSILON = 1e-06
BLK = ("by", "bz")
BAND = ("nz", "nx", "nc")


def padded_2(cells, sides, width):
    for axis, dim in sides:
        count = lax.axis_size(axis)
        ends = count - 1
        head = lax.slice_in_dim(cells, 0, width, axis=dim)
        tail = lax.slice_in_dim(cells, cells.shape[dim] - width, cells.shape[dim], axis=dim)
        cells = jnp.concatenate(
            [
                lax.ppermute(tail, axis, [(i, (i + 1) % count) for i in range(ends)]),
                cells,
                lax.ppermute(head, axis, [((i + 1) % count, i) for i in range(ends)]),
            ],
            axis=dim,
        )
    return cells


def shards(spectra, live, pair_table):
    home_rows = spectra.shape[0]
    windows = spectra.shape[1]
    bins_dev = spectra.shape[3]
    blocks_total = lax.axis_size(BLK)
    me_block = lax.axis_index(BLK)
    first_row = me_block * home_rows
    channels = blocks_total * home_rows
    values = spectra.astype(jnp.float32)
    real_part = values[:, :, 0, :]
    imag_part = values[:, :, 1, :]
    amplitude = jnp.sqrt(real_part * real_part + imag_part * imag_part)
    padded = padded_2(amplitude, ((BAND, 2),), SMOOTH)
    wide_bins = bins_dev + 2 * SMOOTH
    source_bin = jnp.arange(wide_bins, dtype=jnp.int32)[:, None]
    target_bin = jnp.arange(bins_dev, dtype=jnp.int32)[None, :]
    window_matrix = ((source_bin >= target_bin) & (source_bin <= target_bin + 2 * SMOOTH)).astype(
        jnp.float32
    )
    total = jnp.dot(
        padded.reshape(home_rows * windows, wide_bins),
        window_matrix,
        precision=lax.Precision.HIGHEST,
        preferred_element_type=jnp.float32,
    )
    total = total.reshape(home_rows, windows, bins_dev)
    indices = lax.axis_index(BAND) * bins_dev + jnp.arange(bins_dev, dtype=jnp.int32)
    covered = (
        jnp.minimum(indices + SMOOTH, FREQ_BINS - 1) - jnp.maximum(indices - SMOOTH, 0) + 1
    ).astype(jnp.float32)
    smooth = total / covered
    factor = live.astype(jnp.float32)[:, :, None] / (smooth + EPSILON)
    white = (values * factor[:, :, None, :]).astype(jnp.bfloat16)
    lag_index = 2 * jnp.arange(LAGS, dtype=jnp.int32) + 1 - LAGS
    phase = (lag_index[:, None] * indices[None, :]).astype(jnp.float32) * (math.pi / FREQ_BINS)
    cosine = jnp.cos(phase)[None, :, None, :]
    sine = jnp.sin(phase)[None, :, None, :]
    white_real = white[:, :, 0, :].astype(jnp.float32)[:, None]
    white_imag = white[:, :, 1, :].astype(jnp.float32)[:, None]
    rot_real = white_real * cosine - white_imag * sine
    rot_imag = white_real * sine + white_imag * cosine
    zeta_wide = jnp.pad(
        jnp.stack([rot_real, rot_imag], axis=3).reshape(home_rows * LAGS, windows * 2, bins_dev),
        ((0, 0), (0, 1), (0, 0)),
    ).astype(jnp.bfloat16).reshape(home_rows * LAGS, -1)

    marks = jnp.zeros((home_rows, bins_dev), jnp.bfloat16).at[:, :windows].set(live.astype(jnp.bfloat16))
    parcel = jnp.concatenate([white.reshape(home_rows, windows * 2, bins_dev), marks[:, None]], axis=1)
    slots = parcel.shape[1]
    row_span = exchanged_on_line(parcel, "bz").reshape(-1, slots, bins_dev)
    ring = lax.axis_size("by")
    me_ring = lax.axis_index("by")
    span = row_span.shape[0]
    half = span // 2
    from_lo = shifted(row_span, "by", 1)
    from_hi = shifted(row_span, "by", -1)
    far_lo = shifted(from_lo[:half], "by", 1)
    far_hi = shifted(from_hi[half:], "by", -1)
    gathered = jnp.zeros((channels, slots, bins_dev), jnp.bfloat16)
    for offset, start, piece in (
        (0, 0, row_span), (1, 0, from_hi), (ring - 1, 0, from_lo), (2, 0, far_lo), (2, half, far_hi)
    ):
        place = ((me_ring + offset) % ring) * span + start
        gathered = lax.dynamic_update_slice(gathered, piece, (place, 0, 0))
    product = lax.dot_general(
        zeta_wide,
        gathered.reshape(channels, -1),
        (((1,), (1,)), ((), ())),
        preferred_element_type=jnp.float32,
    )
    count = lax.dot_general(
        live.astype(jnp.float32),
        gathered[:, windows * 2, :windows].astype(jnp.float32),
        (((1,), (1,)), ((), ())),
        precision=lax.Precision.HIGHEST,
        preferred_element_type=jnp.float32,
    )
    keep = jnp.broadcast_to(pair_table[0][:, None], (blocks_total, home_rows)).reshape(channels)
    rows_global = first_row + jnp.arange(home_rows, dtype=jnp.int32)
    columns = jnp.arange(channels, dtype=jnp.int32)
    apart = (rows_global[:, None] != columns[None, :]).astype(jnp.float32)
    weight = keep.astype(jnp.float32)[None, :] * apart / jnp.sqrt(bins_dev * jnp.maximum(count, 1.0))
    result = product.reshape(home_rows, LAGS, channels) * weight[:, None, :]
    return result[None]


def shifted(value, axis, steps):
    count = lax.axis_size(axis)
    return lax.ppermute(value, axis, [(i, (i + steps) % count) for i in range(count)])


def exchanged_on_line(value, axis):
    count = lax.axis_size(axis)
    me = lax.axis_index(axis)
    held = value[None]
    stride = 1
    while stride < count:
        other = lax.ppermute(held, axis, [(i, i ^ stride) for i in range(count)])
        low = (me // stride) % 2 == 0
        held = jnp.concatenate(
            [jnp.where(low, held, other), jnp.where(low, other, held)], axis=0
        )
        stride *= 2
    return held


def solution(mesh):
    blk_size, band_size = mesh.devices.shape
    fine = Mesh(mesh.devices.reshape(4, blk_size // 4, 2, band_size // 4, 2), BLK + BAND)
    in_specs = (P(BLK, None, None, BAND), P(BLK, None), P(BLK, None))
    out_specs = P(BAND, BLK, None, None)
    return jax.shard_map(shards, mesh=fine, in_specs=in_specs, out_specs=out_specs, check_vma=False)
```

```python
import math

import jax
import jax.numpy as jnp
from jax import lax
from jax.sharding import Mesh, PartitionSpec as P

LAGS = 32
FREQ_BINS = 2048
SMOOTH = 32


EPSILON = 1e-06
BLK = ("by", "bz")
BAND = ("nz", "nx", "nc")


def padded_2(cells, sides, width):
    for axis, dim in sides:
        count = lax.axis_size(axis)
        ends = count - 1
        head = lax.slice_in_dim(cells, 0, width, axis=dim)
        tail = lax.slice_in_dim(cells, cells.shape[dim] - width, cells.shape[dim], axis=dim)
        cells = jnp.concatenate(
            [
                lax.ppermute(tail, axis, [(i, (i + 1) % count) for i in range(ends)]),
                cells,
                lax.ppermute(head, axis, [((i + 1) % count, i) for i in range(ends)]),
            ],
            axis=dim,
        )
    return cells


def shards(spectra, live, pair_table):
    home_rows = spectra.shape[0]
    windows = spectra.shape[1]
    bins_dev = spectra.shape[3]
    blocks_total = lax.axis_size(BLK)
    me_block = lax.axis_index(BLK)
    first_row = me_block * home_rows
    channels = blocks_total * home_rows
    values = spectra.astype(jnp.float32)
    real_part = values[:, :, 0, :]
    imag_part = values[:, :, 1, :]
    amplitude = jnp.sqrt(real_part * real_part + imag_part * imag_part)
    padded = padded_2(amplitude, ((BAND, 2),), SMOOTH)
    wide_bins = bins_dev + 2 * SMOOTH
    source_bin = jnp.arange(wide_bins, dtype=jnp.int32)[:, None]
    target_bin = jnp.arange(bins_dev, dtype=jnp.int32)[None, :]
    window_matrix = ((source_bin >= target_bin) & (source_bin <= target_bin + 2 * SMOOTH)).astype(
        jnp.float32
    )
    total = jnp.dot(
        padded.reshape(home_rows * windows, wide_bins),
        window_matrix,
        precision=lax.Precision.HIGHEST,
        preferred_element_type=jnp.float32,
    )
    total = total.reshape(home_rows, windows, bins_dev)
    indices = lax.axis_index(BAND) * bins_dev + jnp.arange(bins_dev, dtype=jnp.int32)
    covered = (
        jnp.minimum(indices + SMOOTH, FREQ_BINS - 1) - jnp.maximum(indices - SMOOTH, 0) + 1
    ).astype(jnp.float32)
    smooth = total / covered
    factor = live.astype(jnp.float32)[:, :, None] / (smooth + EPSILON)
    white = (values * factor[:, :, None, :]).astype(jnp.bfloat16)
    lag_index = 2 * jnp.arange(LAGS, dtype=jnp.int32) + 1 - LAGS
    phase = (lag_index[:, None] * indices[None, :]).astype(jnp.float32) * (math.pi / FREQ_BINS)
    cosine = jnp.cos(phase)[None, :, None, :]
    sine = jnp.sin(phase)[None, :, None, :]
    white_real = white[:, :, 0, :].astype(jnp.float32)[:, None]
    white_imag = white[:, :, 1, :].astype(jnp.float32)[:, None]
    rot_real = white_real * cosine - white_imag * sine
    rot_imag = white_real * sine + white_imag * cosine
    zeta_wide = jnp.pad(
        jnp.stack([rot_real, rot_imag], axis=3).reshape(home_rows * LAGS, windows * 2, bins_dev),
        ((0, 0), (0, 1), (0, 0)),
    ).astype(jnp.bfloat16).reshape(home_rows * LAGS, -1)

    marks = jnp.zeros((home_rows, bins_dev), jnp.bfloat16).at[:, :windows].set(live.astype(jnp.bfloat16))
    parcel = jnp.concatenate([white.reshape(home_rows, windows * 2, bins_dev), marks[:, None]], axis=1)
    slots = parcel.shape[1]
    gathered = spread(parcel, "bz")
    gathered = spread(gathered.reshape(-1, slots, bins_dev), "by").reshape(channels, slots, bins_dev)
    product = lax.dot_general(
        zeta_wide,
        gathered.reshape(channels, -1),
        (((1,), (1,)), ((), ())),
        preferred_element_type=jnp.float32,
    )
    count = lax.dot_general(
        live.astype(jnp.float32),
        gathered[:, windows * 2, :windows].astype(jnp.float32),
        (((1,), (1,)), ((), ())),
        precision=lax.Precision.HIGHEST,
        preferred_element_type=jnp.float32,
    )
    keep = jnp.broadcast_to(pair_table[0][:, None], (blocks_total, home_rows)).reshape(channels)
    rows_global = first_row + jnp.arange(home_rows, dtype=jnp.int32)
    columns = jnp.arange(channels, dtype=jnp.int32)
    apart = (rows_global[:, None] != columns[None, :]).astype(jnp.float32)
    weight = keep.astype(jnp.float32)[None, :] * apart / jnp.sqrt(bins_dev * jnp.maximum(count, 1.0))
    result = product.reshape(home_rows, LAGS, channels) * weight[:, None, :]
    return result[None]


def spread(value, axis):
    count = lax.axis_size(axis)
    copies = jnp.broadcast_to(value[None], (count,) + value.shape)
    return lax.all_to_all(copies, axis, 0, 0)


def solution(mesh):
    blk_size, band_size = mesh.devices.shape
    fine = Mesh(mesh.devices.reshape(4, blk_size // 4, 2, band_size // 4, 2), BLK + BAND)
    in_specs = (P(BLK, None, None, BAND), P(BLK, None), P(BLK, None))
    out_specs = P(BAND, BLK, None, None)
    return jax.shard_map(shards, mesh=fine, in_specs=in_specs, out_specs=out_specs, check_vma=False)
```

```python
import math

import jax
import jax.numpy as jnp
from jax import lax
from jax.experimental import pallas as pl
from jax.sharding import Mesh, PartitionSpec as P

LAGS = 32
FREQ_BINS = 2048
SMOOTH = 32


EPSILON = 1e-06
BLK = ("by", "bz")
BAND = ("nz", "nx", "nc")


def padded_2(cells, sides, width):
    for axis, dim in sides:
        count = lax.axis_size(axis)
        ends = count - 1
        head = lax.slice_in_dim(cells, 0, width, axis=dim)
        tail = lax.slice_in_dim(cells, cells.shape[dim] - width, cells.shape[dim], axis=dim)
        cells = jnp.concatenate(
            [
                lax.ppermute(tail, axis, [(i, (i + 1) % count) for i in range(ends)]),
                cells,
                lax.ppermute(head, axis, [((i + 1) % count, i) for i in range(ends)]),
            ],
            axis=dim,
        )
    return cells


def shards(spectra, live, pair_table):
    home_rows = spectra.shape[0]
    windows = spectra.shape[1]
    bins_dev = spectra.shape[3]
    blocks_total = lax.axis_size(BLK)
    me_block = lax.axis_index(BLK)
    first_row = me_block * home_rows
    channels = blocks_total * home_rows
    values = spectra.astype(jnp.float32)
    real_part = values[:, :, 0, :]
    imag_part = values[:, :, 1, :]
    amplitude = jnp.sqrt(real_part * real_part + imag_part * imag_part)
    padded = padded_2(amplitude, ((BAND, 2),), SMOOTH)
    wide_bins = bins_dev + 2 * SMOOTH
    source_bin = jnp.arange(wide_bins, dtype=jnp.int32)[:, None]
    target_bin = jnp.arange(bins_dev, dtype=jnp.int32)[None, :]
    window_matrix = ((source_bin >= target_bin) & (source_bin <= target_bin + 2 * SMOOTH)).astype(
        jnp.float32
    )
    total = jnp.dot(
        padded.reshape(home_rows * windows, wide_bins),
        window_matrix,
        precision=lax.Precision.HIGHEST,
        preferred_element_type=jnp.float32,
    )
    total = total.reshape(home_rows, windows, bins_dev)
    indices = lax.axis_index(BAND) * bins_dev + jnp.arange(bins_dev, dtype=jnp.int32)
    covered = (
        jnp.minimum(indices + SMOOTH, FREQ_BINS - 1) - jnp.maximum(indices - SMOOTH, 0) + 1
    ).astype(jnp.float32)
    smooth = total / covered
    factor = live.astype(jnp.float32)[:, :, None] / (smooth + EPSILON)
    white = (values * factor[:, :, None, :]).astype(jnp.bfloat16)
    lag_index = 2 * jnp.arange(LAGS, dtype=jnp.int32) + 1 - LAGS
    phase = (lag_index[:, None] * indices[None, :]).astype(jnp.float32) * (math.pi / FREQ_BINS)
    cosine = jnp.cos(phase)[None, :, None, :]
    sine = jnp.sin(phase)[None, :, None, :]
    white_real = white[:, :, 0, :].astype(jnp.float32)[:, None]
    white_imag = white[:, :, 1, :].astype(jnp.float32)[:, None]
    rot_real = white_real * cosine - white_imag * sine
    rot_imag = white_real * sine + white_imag * cosine
    rotated = jnp.stack([rot_real, rot_imag], axis=3).reshape(home_rows * LAGS, -1)
    zeta_wide = jnp.concatenate(
        [rotated, jnp.zeros((home_rows * LAGS, bins_dev), jnp.float32)], axis=1
    ).astype(jnp.bfloat16)

    marks = jnp.zeros((home_rows, bins_dev), jnp.bfloat16).at[:, :windows].set(live.astype(jnp.bfloat16))
    parcel = jnp.concatenate([white.reshape(home_rows, -1), marks], axis=1)
    width = parcel.shape[1]
    gathered = spread(parcel, "bz").reshape(-1, width)
    gathered = spread(gathered, "by").reshape(channels, width)
    count = lax.dot_general(
        live.astype(jnp.float32),
        gathered[:, width - bins_dev : width - bins_dev + windows].astype(jnp.float32),
        (((1,), (1,)), ((), ())),
        precision=lax.Precision.HIGHEST,
        preferred_element_type=jnp.float32,
    )
    keep = jnp.broadcast_to(pair_table[0][:, None], (blocks_total, home_rows)).reshape(channels)
    rows_global = first_row + jnp.arange(home_rows, dtype=jnp.int32)
    columns = jnp.arange(channels, dtype=jnp.int32)
    apart = (rows_global[:, None] != columns[None, :]).astype(jnp.float32)
    weight = keep.astype(jnp.float32)[None, :] * apart / jnp.sqrt(bins_dev * jnp.maximum(count, 1.0))
    return correlated(zeta_wide, gathered, weight, home_rows)[None]


def correlate_block(zeta_ref, chunk_ref, weight_ref, out_ref):
    product = lax.dot_general(
        zeta_ref[...],
        chunk_ref[...],
        (((1,), (1,)), ((), ())),
        preferred_element_type=jnp.float32,
    )
    rows, lags, span = out_ref.shape
    out_ref[...] = product.reshape(rows, lags, span) * weight_ref[...][:, None, :]


def correlated(zeta_wide, gathered, weight, rows):
    depth, width = zeta_wide.shape
    channels = gathered.shape[0]
    span = 256
    return pl.pallas_call(
        correlate_block,
        grid=(channels // span,),
        in_specs=[
            pl.BlockSpec((depth, width), lambda j: (0, 0)),
            pl.BlockSpec((span, width), lambda j: (j, 0)),
            pl.BlockSpec((rows, span), lambda j: (0, j)),
        ],
        out_specs=pl.BlockSpec((rows, depth // rows, span), lambda j: (0, 0, j)),
        out_shape=jax.ShapeDtypeStruct((rows, depth // rows, channels), jnp.float32),
        cost_estimate=pl.CostEstimate(
            flops=2 * depth * width * channels,
            transcendentals=0,
            bytes_accessed=2 * depth * width + 2 * channels * width + 4 * depth * channels,
        ),
    )(zeta_wide, gathered, weight)


def spread(value, axis):
    count = lax.axis_size(axis)
    copies = jnp.broadcast_to(value[None], (count,) + value.shape)
    return lax.all_to_all(copies, axis, 0, 0)


def solution(mesh):
    blk_size, band_size = mesh.devices.shape
    fine = Mesh(mesh.devices.reshape(4, blk_size // 4, 2, band_size // 4, 2), BLK + BAND)
    in_specs = (P(BLK, None, None, BAND), P(BLK, None), P(BLK, None))
    out_specs = P(BAND, BLK, None, None)
    return jax.shard_map(shards, mesh=fine, in_specs=in_specs, out_specs=out_specs, check_vma=False)
```

```python
import math

import jax
import jax.numpy as jnp
from jax import lax
from jax.experimental import pallas as pl
from jax.sharding import Mesh, PartitionSpec as P

LAGS = 32
FREQ_BINS = 2048
SMOOTH = 32


EPSILON = 1e-06
BLK = ("by", "bz")
BAND = ("nz", "nx", "nc")


def padded_2(cells, sides, width):
    for axis, dim in sides:
        count = lax.axis_size(axis)
        ends = count - 1
        head = lax.slice_in_dim(cells, 0, width, axis=dim)
        tail = lax.slice_in_dim(cells, cells.shape[dim] - width, cells.shape[dim], axis=dim)
        cells = jnp.concatenate(
            [
                lax.ppermute(tail, axis, [(i, (i + 1) % count) for i in range(ends)]),
                cells,
                lax.ppermute(head, axis, [((i + 1) % count, i) for i in range(ends)]),
            ],
            axis=dim,
        )
    return cells


def shards(spectra, live, pair_table):
    home_rows = spectra.shape[0]
    windows = spectra.shape[1]
    bins_dev = spectra.shape[3]
    blocks_total = lax.axis_size(BLK)
    me_block = lax.axis_index(BLK)
    first_row = me_block * home_rows
    channels = blocks_total * home_rows
    values = spectra.astype(jnp.float32)
    real_part = values[:, :, 0, :]
    imag_part = values[:, :, 1, :]
    amplitude = jnp.sqrt(real_part * real_part + imag_part * imag_part)
    padded = padded_2(amplitude, ((BAND, 2),), SMOOTH)
    wide_bins = bins_dev + 2 * SMOOTH
    source_bin = jnp.arange(wide_bins, dtype=jnp.int32)[:, None]
    target_bin = jnp.arange(bins_dev, dtype=jnp.int32)[None, :]
    window_matrix = ((source_bin >= target_bin) & (source_bin <= target_bin + 2 * SMOOTH)).astype(
        jnp.float32
    )
    total = jnp.dot(
        padded.reshape(home_rows * windows, wide_bins),
        window_matrix,
        precision=lax.Precision.HIGHEST,
        preferred_element_type=jnp.float32,
    )
    total = total.reshape(home_rows, windows, bins_dev)
    indices = lax.axis_index(BAND) * bins_dev + jnp.arange(bins_dev, dtype=jnp.int32)
    covered = (
        jnp.minimum(indices + SMOOTH, FREQ_BINS - 1) - jnp.maximum(indices - SMOOTH, 0) + 1
    ).astype(jnp.float32)
    smooth = total / covered
    factor = live.astype(jnp.float32)[:, :, None] / (smooth + EPSILON)
    white = (values * factor[:, :, None, :]).astype(jnp.bfloat16)
    lag_index = 2 * jnp.arange(LAGS, dtype=jnp.int32) + 1 - LAGS
    phase = (lag_index[:, None] * indices[None, :]).astype(jnp.float32) * (math.pi / FREQ_BINS)
    cosine = jnp.cos(phase)[None, :, None, :]
    sine = jnp.sin(phase)[None, :, None, :]
    white_real = white[:, :, 0, :].astype(jnp.float32)[:, None]
    white_imag = white[:, :, 1, :].astype(jnp.float32)[:, None]
    rot_real = white_real * cosine - white_imag * sine
    rot_imag = white_real * sine + white_imag * cosine
    rotated = jnp.stack([rot_real, rot_imag], axis=3).reshape(home_rows * LAGS, -1)
    zeta_wide = jnp.concatenate(
        [rotated, jnp.zeros((home_rows * LAGS, bins_dev), jnp.float32)], axis=1
    ).astype(jnp.bfloat16)

    marks = jnp.zeros((home_rows, bins_dev), jnp.bfloat16).at[:, :windows].set(live.astype(jnp.bfloat16))
    parcel = jnp.concatenate([white.reshape(home_rows, -1), marks], axis=1)
    width = parcel.shape[1]
    gathered = spread(parcel, "bz").reshape(-1, width)
    gathered = spread(gathered, "by").reshape(channels, width)
    keep = jnp.broadcast_to(pair_table[0][:, None], (blocks_total, home_rows)).reshape(channels)
    rows_global = first_row + jnp.arange(home_rows, dtype=jnp.int32)
    columns = jnp.arange(channels, dtype=jnp.int32)
    apart = (rows_global[:, None] != columns[None, :]).astype(jnp.float32)
    kept = keep.astype(jnp.float32)[None, :] * apart
    return correlated(zeta_wide, gathered, kept, marks, home_rows)[None]


def correlate_block(zeta_ref, chunk_ref, kept_ref, marks_ref, out_ref):
    rows, lags, span = out_ref.shape
    depth, width = zeta_ref.shape
    bins = marks_ref.shape[1]
    product = lax.dot_general(
        zeta_ref[...],
        chunk_ref[...],
        (((1,), (1,)), ((), ())),
        preferred_element_type=jnp.float32,
    )
    count = lax.dot_general(
        marks_ref[...],
        chunk_ref[:, width - bins :],
        (((1,), (1,)), ((), ())),
        preferred_element_type=jnp.float32,
    )
    weight = kept_ref[...] / jnp.sqrt(bins * jnp.maximum(count, 1.0))
    out_ref[...] = product.reshape(rows, lags, span) * weight[:, None, :]


def correlated(zeta_wide, gathered, kept, marks, rows):
    depth, width = zeta_wide.shape
    channels = gathered.shape[0]
    bins = marks.shape[1]
    span = 512
    return pl.pallas_call(
        correlate_block,
        grid=(channels // span,),
        in_specs=[
            pl.BlockSpec((depth, width), lambda j: (0, 0)),
            pl.BlockSpec((span, width), lambda j: (j, 0)),
            pl.BlockSpec((rows, span), lambda j: (0, j)),
            pl.BlockSpec((rows, bins), lambda j: (0, 0)),
        ],
        out_specs=pl.BlockSpec((rows, depth // rows, span), lambda j: (0, 0, j)),
        out_shape=jax.ShapeDtypeStruct((rows, depth // rows, channels), jnp.float32),
        cost_estimate=pl.CostEstimate(
            flops=2 * depth * width * channels,
            transcendentals=0,
            bytes_accessed=2 * depth * width + 2 * channels * width + 4 * depth * channels,
        ),
    )(zeta_wide, gathered, kept, marks)


def spread(value, axis):
    count = lax.axis_size(axis)
    copies = jnp.broadcast_to(value[None], (count,) + value.shape)
    return lax.all_to_all(copies, axis, 0, 0)


def solution(mesh):
    blk_size, band_size = mesh.devices.shape
    fine = Mesh(mesh.devices.reshape(4, blk_size // 4, 2, band_size // 4, 2), BLK + BAND)
    in_specs = (P(BLK, None, None, BAND), P(BLK, None), P(BLK, None))
    out_specs = P(BAND, BLK, None, None)
    return jax.shard_map(shards, mesh=fine, in_specs=in_specs, out_specs=out_specs, check_vma=False)
```

```python
import math

import jax
import jax.numpy as jnp
from jax import lax
from jax.experimental import pallas as pl
from jax.sharding import Mesh, PartitionSpec as P

LAGS = 32
FREQ_BINS = 2048
SMOOTH = 32


EPSILON = 1e-06
BLK = ("by", "bz")
BAND = ("nz", "nx", "nc")


def padded_2(cells, sides, width):
    for axis, dim in sides:
        count = lax.axis_size(axis)
        ends = count - 1
        head = lax.slice_in_dim(cells, 0, width, axis=dim)
        tail = lax.slice_in_dim(cells, cells.shape[dim] - width, cells.shape[dim], axis=dim)
        cells = jnp.concatenate(
            [
                lax.ppermute(tail, axis, [(i, (i + 1) % count) for i in range(ends)]),
                cells,
                lax.ppermute(head, axis, [((i + 1) % count, i) for i in range(ends)]),
            ],
            axis=dim,
        )
    return cells


def shards(spectra, live, pair_table):
    home_rows = spectra.shape[0]
    windows = spectra.shape[1]
    bins_dev = spectra.shape[3]
    blocks_total = lax.axis_size(BLK)
    me_block = lax.axis_index(BLK)
    first_row = me_block * home_rows
    channels = blocks_total * home_rows
    values = spectra.astype(jnp.float32)
    real_part = values[:, :, 0, :]
    imag_part = values[:, :, 1, :]
    amplitude = jnp.sqrt(real_part * real_part + imag_part * imag_part)
    padded = padded_2(amplitude, ((BAND, 2),), SMOOTH)
    wide_bins = bins_dev + 2 * SMOOTH
    source_bin = jnp.arange(wide_bins, dtype=jnp.int32)[:, None]
    target_bin = jnp.arange(bins_dev, dtype=jnp.int32)[None, :]
    window_matrix = ((source_bin >= target_bin) & (source_bin <= target_bin + 2 * SMOOTH)).astype(
        jnp.float32
    )
    total = jnp.dot(
        padded.reshape(home_rows * windows, wide_bins),
        window_matrix,
        precision=lax.Precision.HIGHEST,
        preferred_element_type=jnp.float32,
    )
    total = total.reshape(home_rows, windows, bins_dev)
    indices = lax.axis_index(BAND) * bins_dev + jnp.arange(bins_dev, dtype=jnp.int32)
    covered = (
        jnp.minimum(indices + SMOOTH, FREQ_BINS - 1) - jnp.maximum(indices - SMOOTH, 0) + 1
    ).astype(jnp.float32)
    smooth = total / covered
    factor = live.astype(jnp.float32)[:, :, None] / (smooth + EPSILON)
    white = (values * factor[:, :, None, :]).astype(jnp.bfloat16)
    lag_index = 2 * jnp.arange(LAGS, dtype=jnp.int32) + 1 - LAGS
    phase = (lag_index[:, None] * indices[None, :]).astype(jnp.float32) * (math.pi / FREQ_BINS)
    cosine = jnp.cos(phase)[None, :, None, :]
    sine = jnp.sin(phase)[None, :, None, :]
    white_real = white[:, :, 0, :].astype(jnp.float32)[:, None]
    white_imag = white[:, :, 1, :].astype(jnp.float32)[:, None]
    rot_real = white_real * cosine - white_imag * sine
    rot_imag = white_real * sine + white_imag * cosine
    zeta = (
        jnp.stack([rot_real, rot_imag], axis=3).astype(jnp.bfloat16).reshape(home_rows * LAGS, -1)
    )

    marks = jnp.zeros((home_rows, bins_dev), jnp.bfloat16).at[:, :windows].set(live.astype(jnp.bfloat16))
    parcel = jnp.concatenate([white.reshape(home_rows, -1), marks], axis=1)
    width = parcel.shape[1]
    line = spread(parcel, "bz")
    span = line.shape[0] * home_rows
    line_marks = jnp.transpose(line[:, :, width - bins_dev : width - bins_dev + windows], (2, 0, 1))
    packed = jnp.concatenate(
        [
            line[:, :, : width - bins_dev].reshape(span, -1),
            line_marks.reshape(1, -1).astype(jnp.bfloat16),
            jnp.zeros((15, windows * span), jnp.bfloat16),
        ],
        axis=0,
    )
    gathered = spread(packed, "by")
    keep = jnp.broadcast_to(pair_table[0][:, None], (blocks_total, home_rows)).reshape(channels)
    rows_global = first_row + jnp.arange(home_rows, dtype=jnp.int32)
    columns = jnp.arange(channels, dtype=jnp.int32)
    apart = (rows_global[:, None] != columns[None, :]).astype(jnp.float32)
    kept = keep.astype(jnp.float32)[None, :] * apart
    return correlated(zeta, gathered, kept, live.astype(jnp.float32), span)[None]


def correlate_block(zeta_ref, chunk_ref, marks_ref, kept_ref, live_ref, out_ref):
    rows, lags, span = out_ref.shape
    product = lax.dot_general(
        zeta_ref[...],
        chunk_ref[0],
        (((1,), (1,)), ((), ())),
        preferred_element_type=jnp.float32,
    )
    marks = marks_ref[0, 0:1, :].astype(jnp.float32)
    count = jnp.zeros((rows, span), jnp.float32)
    for w in range(live_ref.shape[1]):
        count = count + live_ref[:, w : w + 1] * marks[:, w * span : (w + 1) * span]
    weight = kept_ref[...] / jnp.sqrt(chunk_ref.shape[2] // (live_ref.shape[1] * 2) * jnp.maximum(count, 1.0))
    out_ref[...] = product.reshape(rows, lags, span) * weight[:, None, :]


def correlated(zeta, gathered, kept, live, span):
    depth, width = zeta.shape
    ring, height, _ = gathered.shape
    rows, windows = live.shape
    channels = ring * span
    tail = height - span
    return pl.pallas_call(
        correlate_block,
        grid=(ring,),
        in_specs=[
            pl.BlockSpec((depth, width), lambda j: (0, 0)),
            pl.BlockSpec((1, span, width), lambda j: (j, 0, 0)),
            pl.BlockSpec((1, tail, width), lambda j: (j, span // tail, 0)),
            pl.BlockSpec((rows, span), lambda j: (0, j)),
            pl.BlockSpec((rows, windows), lambda j: (0, 0)),
        ],
        out_specs=pl.BlockSpec((rows, depth // rows, span), lambda j: (0, 0, j)),
        out_shape=jax.ShapeDtypeStruct((rows, depth // rows, channels), jnp.float32),
        cost_estimate=pl.CostEstimate(
            flops=2 * depth * width * channels,
            transcendentals=0,
            bytes_accessed=2 * depth * width + 2 * channels * width + 4 * depth * channels,
        ),
    )(zeta, gathered, gathered, kept, live)


def spread(value, axis):
    count = lax.axis_size(axis)
    copies = jnp.broadcast_to(value[None], (count,) + value.shape)
    return lax.all_to_all(copies, axis, 0, 0)


def solution(mesh):
    blk_size, band_size = mesh.devices.shape
    fine = Mesh(mesh.devices.reshape(4, blk_size // 4, 2, band_size // 4, 2), BLK + BAND)
    in_specs = (P(BLK, None, None, BAND), P(BLK, None), P(BLK, None))
    out_specs = P(BAND, BLK, None, None)
    return jax.shard_map(shards, mesh=fine, in_specs=in_specs, out_specs=out_specs, check_vma=False)
```

```python
import math

import jax
import jax.numpy as jnp
from jax import lax
from jax.experimental import pallas as pl
from jax.sharding import Mesh, PartitionSpec as P

LAGS = 32
FREQ_BINS = 2048
SMOOTH = 32


EPSILON = 1e-06
BLK = ("by", "bz")
BAND = ("nz", "nx", "nc")


def padded_2(cells, sides, width):
    for axis, dim in sides:
        count = lax.axis_size(axis)
        ends = count - 1
        head = lax.slice_in_dim(cells, 0, width, axis=dim)
        tail = lax.slice_in_dim(cells, cells.shape[dim] - width, cells.shape[dim], axis=dim)
        cells = jnp.concatenate(
            [
                lax.ppermute(tail, axis, [(i, (i + 1) % count) for i in range(ends)]),
                cells,
                lax.ppermute(head, axis, [((i + 1) % count, i) for i in range(ends)]),
            ],
            axis=dim,
        )
    return cells


def shards(spectra, live, pair_table):
    home_rows = spectra.shape[0]
    windows = spectra.shape[1]
    bins_dev = spectra.shape[3]
    blocks_total = lax.axis_size(BLK)
    me_block = lax.axis_index(BLK)
    first_row = me_block * home_rows
    channels = blocks_total * home_rows
    values = spectra.astype(jnp.float32)
    real_part = values[:, :, 0, :]
    imag_part = values[:, :, 1, :]
    amplitude = jnp.sqrt(real_part * real_part + imag_part * imag_part)
    padded = padded_2(amplitude, ((BAND, 2),), SMOOTH)
    wide_bins = bins_dev + 2 * SMOOTH
    source_bin = jnp.arange(wide_bins, dtype=jnp.int32)[:, None]
    target_bin = jnp.arange(bins_dev, dtype=jnp.int32)[None, :]
    window_matrix = ((source_bin >= target_bin) & (source_bin <= target_bin + 2 * SMOOTH)).astype(
        jnp.float32
    )
    total = jnp.dot(
        padded.reshape(home_rows * windows, wide_bins),
        window_matrix,
        precision=lax.Precision.HIGHEST,
        preferred_element_type=jnp.float32,
    )
    total = total.reshape(home_rows, windows, bins_dev)
    indices = lax.axis_index(BAND) * bins_dev + jnp.arange(bins_dev, dtype=jnp.int32)
    covered = (
        jnp.minimum(indices + SMOOTH, FREQ_BINS - 1) - jnp.maximum(indices - SMOOTH, 0) + 1
    ).astype(jnp.float32)
    smooth = total / covered
    factor = live.astype(jnp.float32)[:, :, None] / (smooth + EPSILON)
    white = (values * factor[:, :, None, :]).astype(jnp.bfloat16)
    lag_index = 2 * jnp.arange(LAGS, dtype=jnp.int32) + 1 - LAGS
    phase = (lag_index[:, None] * indices[None, :]).astype(jnp.float32) * (math.pi / FREQ_BINS)
    cosine = jnp.cos(phase)[None, :, None, :]
    sine = jnp.sin(phase)[None, :, None, :]
    white_real = white[:, :, 0, :].astype(jnp.float32)[:, None]
    white_imag = white[:, :, 1, :].astype(jnp.float32)[:, None]
    rot_real = white_real * cosine - white_imag * sine
    rot_imag = white_real * sine + white_imag * cosine
    zeta = (
        jnp.stack([rot_real, rot_imag], axis=3).astype(jnp.bfloat16).reshape(home_rows * LAGS, -1)
    )

    lanes = home_rows * windows
    parcel = jnp.concatenate(
        [
            white.reshape(-1, bins_dev),
            live.astype(jnp.bfloat16).reshape(1, lanes),
            jnp.zeros((15, lanes), jnp.bfloat16),
        ],
        axis=0,
    )
    line = spread(parcel, "bz")
    depth = white.shape[1] * white.shape[2]
    span = line.shape[0] * home_rows
    line_marks = jnp.transpose(
        line[:, depth * home_rows, :].reshape(-1, home_rows, windows), (2, 0, 1)
    )
    packed = jnp.concatenate(
        [
            line[:, : depth * home_rows, :].reshape(span, -1),
            line_marks.reshape(1, -1),
            jnp.zeros((15, windows * span), jnp.bfloat16),
        ],
        axis=0,
    )
    gathered = spread(packed, "by")
    keep = jnp.broadcast_to(pair_table[0][:, None], (blocks_total, home_rows)).reshape(channels)
    rows_global = first_row + jnp.arange(home_rows, dtype=jnp.int32)
    columns = jnp.arange(channels, dtype=jnp.int32)
    apart = (rows_global[:, None] != columns[None, :]).astype(jnp.float32)
    kept = keep.astype(jnp.float32)[None, :] * apart
    return correlated(zeta, gathered, kept, live.astype(jnp.float32), span)[None]


def correlate_block(zeta_ref, chunk_ref, marks_ref, kept_ref, live_ref, out_ref):
    rows, lags, span = out_ref.shape
    product = lax.dot_general(
        zeta_ref[...],
        chunk_ref[0],
        (((1,), (1,)), ((), ())),
        preferred_element_type=jnp.float32,
    )
    marks = marks_ref[0, 0:1, :].astype(jnp.float32)
    count = jnp.zeros((rows, span), jnp.float32)
    for w in range(live_ref.shape[1]):
        count = count + live_ref[:, w : w + 1] * marks[:, w * span : (w + 1) * span]
    weight = kept_ref[...] / jnp.sqrt(chunk_ref.shape[2] // (live_ref.shape[1] * 2) * jnp.maximum(count, 1.0))
    out_ref[...] = product.reshape(rows, lags, span) * weight[:, None, :]


def correlated(zeta, gathered, kept, live, span):
    depth, width = zeta.shape
    ring, height, _ = gathered.shape
    rows, windows = live.shape
    channels = ring * span
    tail = height - span
    return pl.pallas_call(
        correlate_block,
        grid=(ring,),
        in_specs=[
            pl.BlockSpec((depth, width), lambda j: (0, 0)),
            pl.BlockSpec((1, span, width), lambda j: (j, 0, 0)),
            pl.BlockSpec((1, tail, width), lambda j: (j, span // tail, 0)),
            pl.BlockSpec((rows, span), lambda j: (0, j)),
            pl.BlockSpec((rows, windows), lambda j: (0, 0)),
        ],
        out_specs=pl.BlockSpec((rows, depth // rows, span), lambda j: (0, 0, j)),
        out_shape=jax.ShapeDtypeStruct((rows, depth // rows, channels), jnp.float32),
        cost_estimate=pl.CostEstimate(
            flops=2 * depth * width * channels,
            transcendentals=0,
            bytes_accessed=2 * depth * width + 2 * channels * width + 4 * depth * channels,
        ),
    )(zeta, gathered, gathered, kept, live)


def spread(value, axis):
    count = lax.axis_size(axis)
    copies = jnp.broadcast_to(value[None], (count,) + value.shape)
    return lax.all_to_all(copies, axis, 0, 0)


def solution(mesh):
    blk_size, band_size = mesh.devices.shape
    fine = Mesh(mesh.devices.reshape(4, blk_size // 4, 2, band_size // 4, 2), BLK + BAND)
    in_specs = (P(BLK, None, None, BAND), P(BLK, None), P(BLK, None))
    out_specs = P(BAND, BLK, None, None)
    return jax.shard_map(shards, mesh=fine, in_specs=in_specs, out_specs=out_specs, check_vma=False)
```

```python
import math

import jax
import jax.numpy as jnp
from jax import lax
from jax.experimental import pallas as pl
from jax.sharding import Mesh, PartitionSpec as P

LAGS = 32
FREQ_BINS = 2048
SMOOTH = 32


EPSILON = 1e-06
BLK = ("by", "bz")
BAND = ("nz", "nx", "nc")


def padded_2(cells, sides, width):
    for axis, dim in sides:
        count = lax.axis_size(axis)
        ends = count - 1
        head = lax.slice_in_dim(cells, 0, width, axis=dim)
        tail = lax.slice_in_dim(cells, cells.shape[dim] - width, cells.shape[dim], axis=dim)
        cells = jnp.concatenate(
            [
                lax.ppermute(tail, axis, [(i, (i + 1) % count) for i in range(ends)]),
                cells,
                lax.ppermute(head, axis, [((i + 1) % count, i) for i in range(ends)]),
            ],
            axis=dim,
        )
    return cells


def shards(spectra, live, pair_table):
    home_rows = spectra.shape[0]
    windows = spectra.shape[1]
    bins_dev = spectra.shape[3]
    blocks_total = lax.axis_size(BLK)
    me_block = lax.axis_index(BLK)
    first_row = me_block * home_rows
    channels = blocks_total * home_rows
    values = spectra.astype(jnp.float32)
    real_part = values[:, :, 0, :]
    imag_part = values[:, :, 1, :]
    amplitude = jnp.sqrt(real_part * real_part + imag_part * imag_part)
    padded = padded_2(amplitude, ((BAND, 2),), SMOOTH)
    wide_bins = bins_dev + 2 * SMOOTH
    source_bin = jnp.arange(wide_bins, dtype=jnp.int32)[:, None]
    target_bin = jnp.arange(bins_dev, dtype=jnp.int32)[None, :]
    window_matrix = ((source_bin >= target_bin) & (source_bin <= target_bin + 2 * SMOOTH)).astype(
        jnp.float32
    )
    total = jnp.dot(
        padded.reshape(home_rows * windows, wide_bins),
        window_matrix,
        precision=lax.Precision.HIGHEST,
        preferred_element_type=jnp.float32,
    )
    total = total.reshape(home_rows, windows, bins_dev)
    indices = lax.axis_index(BAND) * bins_dev + jnp.arange(bins_dev, dtype=jnp.int32)
    covered = (
        jnp.minimum(indices + SMOOTH, FREQ_BINS - 1) - jnp.maximum(indices - SMOOTH, 0) + 1
    ).astype(jnp.float32)
    smooth = total / covered
    factor = live.astype(jnp.float32)[:, :, None] / (smooth + EPSILON)
    white = (values * factor[:, :, None, :]).astype(jnp.bfloat16)
    lag_index = 2 * jnp.arange(LAGS, dtype=jnp.int32) + 1 - LAGS
    phase = (lag_index[:, None] * indices[None, :]).astype(jnp.float32) * (math.pi / FREQ_BINS)
    cosine = jnp.cos(phase)[None, :, None, :]
    sine = jnp.sin(phase)[None, :, None, :]
    white_real = white[:, :, 0, :].astype(jnp.float32)[:, None]
    white_imag = white[:, :, 1, :].astype(jnp.float32)[:, None]
    rot_real = white_real * cosine - white_imag * sine
    rot_imag = white_real * sine + white_imag * cosine
    zeta = (
        jnp.stack([rot_real, rot_imag], axis=3).astype(jnp.bfloat16).reshape(home_rows * LAGS, -1)
    )

    lanes = home_rows * windows
    parcel = jnp.concatenate(
        [
            white.reshape(-1, bins_dev),
            live.astype(jnp.bfloat16).reshape(1, lanes),
            jnp.zeros((15, lanes), jnp.bfloat16),
        ],
        axis=0,
    )
    line = spread(parcel, "bz")
    depth = white.shape[1] * white.shape[2]
    span = line.shape[0] * home_rows
    line_marks = jnp.transpose(
        line[:, depth * home_rows, :].reshape(-1, home_rows, windows), (2, 0, 1)
    )
    packed = jnp.concatenate(
        [
            line[:, : depth * home_rows, :].reshape(span, -1),
            line_marks.reshape(1, -1),
            jnp.zeros((15, windows * span), jnp.bfloat16),
        ],
        axis=0,
    )
    gathered = spread(packed, "by")
    keep = jnp.broadcast_to(pair_table[0][:, None], (blocks_total, home_rows)).reshape(channels)
    rows_global = first_row + jnp.arange(home_rows, dtype=jnp.int32)
    columns = jnp.arange(channels, dtype=jnp.int32)
    apart = (rows_global[:, None] != columns[None, :]).astype(jnp.float32)
    kept = keep.astype(jnp.float32)[None, :] * apart
    return correlated(zeta, gathered, kept, live.astype(jnp.float32), span)[None]


def correlate_block(zeta_ref, chunk_ref, marks_ref, kept_ref, live_ref, out_ref):
    rows, lags, span = out_ref.shape
    pieces, part, width = chunk_ref.shape
    product = lax.dot_general(
        zeta_ref[...],
        chunk_ref[...].reshape(span, width),
        (((1,), (1,)), ((), ())),
        preferred_element_type=jnp.float32,
    )
    counts = []
    for piece in range(pieces):
        marks = marks_ref[piece, 0:1, :].astype(jnp.float32)
        count = jnp.zeros((rows, part), jnp.float32)
        for w in range(live_ref.shape[1]):
            count = count + live_ref[:, w : w + 1] * marks[:, w * part : (w + 1) * part]
        counts.append(count)
    count = jnp.concatenate(counts, axis=1)
    weight = kept_ref[...] / jnp.sqrt(width // (live_ref.shape[1] * 2) * jnp.maximum(count, 1.0))
    out_ref[...] = product.reshape(rows, lags, span) * weight[:, None, :]


def correlated(zeta, gathered, kept, live, part):
    depth, width = zeta.shape
    ring, height, _ = gathered.shape
    rows, windows = live.shape
    channels = ring * part
    tail = height - part
    pieces = 2
    span = pieces * part
    return pl.pallas_call(
        correlate_block,
        grid=(ring // pieces,),
        in_specs=[
            pl.BlockSpec((depth, width), lambda j: (0, 0)),
            pl.BlockSpec((pieces, part, width), lambda j: (j, 0, 0)),
            pl.BlockSpec((pieces, tail, width), lambda j: (j, part // tail, 0)),
            pl.BlockSpec((rows, span), lambda j: (0, j)),
            pl.BlockSpec((rows, windows), lambda j: (0, 0)),
        ],
        out_specs=pl.BlockSpec((rows, depth // rows, span), lambda j: (0, 0, j)),
        out_shape=jax.ShapeDtypeStruct((rows, depth // rows, channels), jnp.float32),
        cost_estimate=pl.CostEstimate(
            flops=2 * depth * width * channels,
            transcendentals=0,
            bytes_accessed=2 * depth * width + 2 * channels * width + 4 * depth * channels,
        ),
    )(zeta, gathered, gathered, kept, live)


def spread(value, axis):
    count = lax.axis_size(axis)
    copies = jnp.broadcast_to(value[None], (count,) + value.shape)
    return lax.all_to_all(copies, axis, 0, 0)


def solution(mesh):
    blk_size, band_size = mesh.devices.shape
    fine = Mesh(mesh.devices.reshape(4, blk_size // 4, 2, band_size // 4, 2), BLK + BAND)
    in_specs = (P(BLK, None, None, BAND), P(BLK, None), P(BLK, None))
    out_specs = P(BAND, BLK, None, None)
    return jax.shard_map(shards, mesh=fine, in_specs=in_specs, out_specs=out_specs, check_vma=False)
```

```python
import math

import jax
import jax.numpy as jnp
from jax import lax
from jax.experimental import pallas as pl
from jax.experimental.pallas import tpu as pltpu
from jax.sharding import Mesh, PartitionSpec as P

LAGS = 32
FREQ_BINS = 2048
SMOOTH = 32


EPSILON = 1e-06
BLK = ("by", "bz")
BAND = ("nz", "nx", "nc")


def padded_2(cells, sides, width):
    for axis, dim in sides:
        count = lax.axis_size(axis)
        ends = count - 1
        head = lax.slice_in_dim(cells, 0, width, axis=dim)
        tail = lax.slice_in_dim(cells, cells.shape[dim] - width, cells.shape[dim], axis=dim)
        cells = jnp.concatenate(
            [
                lax.ppermute(tail, axis, [(i, (i + 1) % count) for i in range(ends)]),
                cells,
                lax.ppermute(head, axis, [((i + 1) % count, i) for i in range(ends)]),
            ],
            axis=dim,
        )
    return cells


def shards(spectra, live, pair_table):
    home_rows = spectra.shape[0]
    windows = spectra.shape[1]
    bins_dev = spectra.shape[3]
    blocks_total = lax.axis_size(BLK)
    me_block = lax.axis_index(BLK)
    first_row = me_block * home_rows
    channels = blocks_total * home_rows
    values = spectra.astype(jnp.float32)
    real_part = values[:, :, 0, :]
    imag_part = values[:, :, 1, :]
    amplitude = jnp.sqrt(real_part * real_part + imag_part * imag_part)
    padded = padded_2(amplitude, ((BAND, 2),), SMOOTH)
    wide_bins = bins_dev + 2 * SMOOTH
    source_bin = jnp.arange(wide_bins, dtype=jnp.int32)[:, None]
    target_bin = jnp.arange(bins_dev, dtype=jnp.int32)[None, :]
    window_matrix = ((source_bin >= target_bin) & (source_bin <= target_bin + 2 * SMOOTH)).astype(
        jnp.float32
    )
    total = jnp.dot(
        padded.reshape(home_rows * windows, wide_bins),
        window_matrix,
        precision=lax.Precision.HIGHEST,
        preferred_element_type=jnp.float32,
    )
    total = total.reshape(home_rows, windows, bins_dev)
    indices = lax.axis_index(BAND) * bins_dev + jnp.arange(bins_dev, dtype=jnp.int32)
    covered = (
        jnp.minimum(indices + SMOOTH, FREQ_BINS - 1) - jnp.maximum(indices - SMOOTH, 0) + 1
    ).astype(jnp.float32)
    smooth = total / covered
    factor = live.astype(jnp.float32)[:, :, None] / (smooth + EPSILON)
    white = (values * factor[:, :, None, :]).astype(jnp.bfloat16)
    lag_index = 2 * jnp.arange(LAGS, dtype=jnp.int32) + 1 - LAGS
    phase = (lag_index[:, None] * indices[None, :]).astype(jnp.float32) * (math.pi / FREQ_BINS)
    cosine = jnp.cos(phase)[None, :, None, :]
    sine = jnp.sin(phase)[None, :, None, :]
    white_real = white[:, :, 0, :].astype(jnp.float32)[:, None]
    white_imag = white[:, :, 1, :].astype(jnp.float32)[:, None]
    rot_real = white_real * cosine - white_imag * sine
    rot_imag = white_real * sine + white_imag * cosine
    zeta = (
        jnp.stack([rot_real, rot_imag], axis=3).astype(jnp.bfloat16).reshape(home_rows * LAGS, -1)
    )

    lanes = home_rows * windows
    parcel = jnp.concatenate(
        [
            white.reshape(-1, bins_dev),
            live.astype(jnp.bfloat16).reshape(1, lanes),
            jnp.zeros((15, lanes), jnp.bfloat16),
        ],
        axis=0,
    )
    line = spread(parcel, "bz")
    depth = white.shape[1] * white.shape[2]
    span = line.shape[0] * home_rows
    line_marks = jnp.transpose(
        line[:, depth * home_rows, :].reshape(-1, home_rows, windows), (2, 0, 1)
    )
    packed = jnp.concatenate(
        [
            line[:, : depth * home_rows, :].reshape(span, -1),
            line_marks.reshape(1, -1),
            jnp.zeros((15, windows * span), jnp.bfloat16),
        ],
        axis=0,
    )
    gathered = spread(packed, "by")
    keep = jnp.broadcast_to(pair_table[0][:, None], (blocks_total, home_rows)).reshape(channels)
    rows_global = first_row + jnp.arange(home_rows, dtype=jnp.int32)
    columns = jnp.arange(channels, dtype=jnp.int32)
    apart = (rows_global[:, None] != columns[None, :]).astype(jnp.float32)
    kept = keep.astype(jnp.float32)[None, :] * apart
    live_f = live.astype(jnp.float32)
    ring_at = lax.axis_index("by").reshape(1)
    own = correlated(zeta, packed[None], kept, live_f, span, ring_at, 0, None)
    return correlated(zeta, gathered, kept, live_f, span, ring_at, 1, own)[None]


def correlate_block(ring_ref, zeta_ref, chunk_ref, marks_ref, kept_ref, live_ref, *refs):
    out_ref = refs[-1]
    rows, lags, span = out_ref.shape
    product = lax.dot_general(
        zeta_ref[...],
        chunk_ref[0],
        (((1,), (1,)), ((), ())),
        preferred_element_type=jnp.float32,
    )
    marks = marks_ref[0, 0:1, :].astype(jnp.float32)
    count = jnp.zeros((rows, span), jnp.float32)
    for w in range(live_ref.shape[1]):
        count = count + live_ref[:, w : w + 1] * marks[:, w * span : (w + 1) * span]
    weight = kept_ref[...] / jnp.sqrt(chunk_ref.shape[2] // (live_ref.shape[1] * 2) * jnp.maximum(count, 1.0))
    out_ref[...] = product.reshape(rows, lags, span) * weight[:, None, :]


def correlated(zeta, gathered, kept, live, span, ring_at, first, earlier):
    depth, width = zeta.shape
    held, height, _ = gathered.shape
    rows, windows = live.shape
    ring = kept.shape[1] // span
    tail = height - span
    steps = held - first

    def source(s, at):
        return jnp.where(first == 0, 0, (at[0] + first + s) % ring)

    def place(s, at):
        return (at[0] + first + s) % ring

    in_specs = [
        pl.BlockSpec((depth, width), lambda s, at: (0, 0)),
        pl.BlockSpec((1, span, width), lambda s, at: (source(s, at), 0, 0)),
        pl.BlockSpec((1, tail, width), lambda s, at: (source(s, at), span // tail, 0)),
        pl.BlockSpec((rows, span), lambda s, at: (0, place(s, at))),
        pl.BlockSpec((rows, windows), lambda s, at: (0, 0)),
    ]
    operands = [zeta, gathered, gathered, kept, live]
    aliases = {}
    if earlier is not None:
        in_specs.append(pl.BlockSpec(memory_space=pl.ANY))
        operands.append(earlier)
        aliases = {len(operands): 0}
    return pl.pallas_call(
        correlate_block,
        grid_spec=pltpu.PrefetchScalarGridSpec(
            num_scalar_prefetch=1,
            grid=(steps,),
            in_specs=in_specs,
            out_specs=pl.BlockSpec((rows, depth // rows, span), lambda s, at: (0, 0, place(s, at))),
        ),
        out_shape=jax.ShapeDtypeStruct((rows, depth // rows, ring * span), jnp.float32),
        input_output_aliases=aliases,
        cost_estimate=pl.CostEstimate(
            flops=2 * depth * width * span * steps,
            transcendentals=0,
            bytes_accessed=2 * depth * width + 2 * span * width * steps + 4 * depth * span * steps,
        ),
    )(ring_at, *operands)


def spread(value, axis):
    count = lax.axis_size(axis)
    copies = jnp.broadcast_to(value[None], (count,) + value.shape)
    return lax.all_to_all(copies, axis, 0, 0)


def solution(mesh):
    blk_size, band_size = mesh.devices.shape
    fine = Mesh(mesh.devices.reshape(4, blk_size // 4, 2, band_size // 4, 2), BLK + BAND)
    in_specs = (P(BLK, None, None, BAND), P(BLK, None), P(BLK, None))
    out_specs = P(BAND, BLK, None, None)
    return jax.shard_map(shards, mesh=fine, in_specs=in_specs, out_specs=out_specs, check_vma=False)
```
